256 devices in a mesh: dp: 16 (over z, core), group: 16 (over x, y).
Axes of the slice: x: 4, y: 4, z: 8, core: 2. Of those that a mesh axis runs over, the one named last changes fastest.
Arguments:
- hidden_in: bfloat16 [16, 16, 128, 5120], P('dp', 'group'), may hold values from -48 to 48
- gain: float32 [5120], replicated, may hold values from 0.1 to 1.9
- value_weight: bfloat16 [5120, 512], P(('dp', 'group')), may hold values from -0.078125 to 0.078125
- value_cot: bfloat16 [16, 16, 128, 512], P('dp', 'group'), may hold values from -6 to 6
- lengths: int32 [16, 16], P('dp', 'group'), may hold values from 1 to 128, as said below
- rewards: int32 [16, 16], P('dp', 'group'), may hold values from 0 to 3
Outputs:
- values: bfloat16 [16, 16, 128, 512], P('dp', 'group')
- weight_grad: float32 [5120, 512], P(('dp', 'group'))
- gain_grad: float32 [5120], P(('dp', 'group'))
The draws below stay inside these ranges and needn't reach their ends.
Inputs may be any that keep to these rules, and one draw needn't show every extreme that they name: `lengths`: some response has exactly 128 tokens.
All inputs are finite; a program needn't handle non-finite values.
Results may differ from the reference program's by a relative error of at most 0.019.
Values may be sent and summed in bfloat16 or wider, within the bound.
No kernel may reach another device: no remote copies, remote signals or barrier semaphores. Data moves between devices by JAX's collectives and lax.ppermute only.
A program may use at most 64 MiB of HBM per device.

```python
import math
import jax
import jax.numpy as jnp
from jax import lax

D = 5120
KVW = 512
L = 128
PROMPTS = 16
RESP = 16


def draw_hidden_in(key, part):
    subkeys = jax.random.split(key, 3)
    full_shape = (PROMPTS, RESP, L, D)
    column_scale = jnp.exp(jax.random.uniform(subkeys[1], (D,), jnp.float32, math.log(0.3), math.log(3.0)))
    row_scale = jnp.exp(jax.random.uniform(subkeys[2], (PROMPTS, RESP, L, 1), jnp.float32, math.log(0.5), math.log(4.0)))
    entries = jnp.clip(jax.random.normal(subkeys[0], full_shape, jnp.float32), -4.0, 4.0)
    return (entries * column_scale * row_scale).astype(jnp.bfloat16)


def draw_lengths(key, part):
    subkeys = jax.random.split(key, 2)
    drawn = jax.random.randint(subkeys[0], (PROMPTS * RESP,), 1, L + 1)
    chosen = jax.random.randint(subkeys[1], (), 0, PROMPTS * RESP)
    drawn = jnp.where(jnp.arange(PROMPTS * RESP) == chosen, L, drawn)
    return drawn.reshape(PROMPTS, RESP).astype(jnp.int32)


def plant(values, own_key, low, largest):
    longest = values.shape.index(max(values.shape))
    spots = []
    for shift in (0, 1):
        where = [jax.random.randint(jax.random.fold_in(own_key, axis), (), 0, length) for axis, length in enumerate(values.shape)]
        where[longest] = (where[longest] + shift) % values.shape[longest]
        spots.append(tuple(where))
    return values.at[spots[0]].set(low).at[spots[1]].set(largest)


def block_levels(rng, extent, pieces, smallest, top_value):
    def one(axis_at, shards_of):
        steps = jax.random.uniform(jax.random.fold_in(jax.random.fold_in(rng, 6), axis_at), (shards_of,), jnp.float32, smallest / len(pieces), top_value / len(pieces))
        return jnp.repeat(jnp.exp(steps), extent[axis_at] // shards_of).reshape((-1,) + (1,) * (len(extent) - axis_at - 1))

    loudness = one(*pieces[0])
    for cut in pieces[1:]:
        loudness = loudness * one(*cut)
    return loudness


def normal_values(own_key, extent, scale, most, cuts=(), dtype=jnp.bfloat16):
    level = block_levels(own_key, extent, cuts, -0.22, 0.18) if cuts else 1.0
    result = jax.random.normal(own_key, extent, jnp.float32) * scale * level
    return jnp.minimum(jnp.maximum(result, -most), most).astype(dtype)


def setup_inputs(seed: int = 0) -> dict:
    streams_of = jax.random.split(jax.random.key(seed), 7)
    return {
        "hidden_in": draw_hidden_in(jax.random.fold_in(streams_of[6], 71), 0),
        "gain": jnp.clip(1.0 + 0.18 * jax.random.normal(streams_of[1], (D,), jnp.float32), 0.1, 1.9),
        "value_weight": normal_values(streams_of[2], (D, KVW), D ** -0.5, 0.078125, ((0, 256),)),
        "value_cot": normal_values(streams_of[3], (PROMPTS, RESP, L, KVW), 1.0, 6.0, ((0, 16), (1, 16))),
        "lengths": draw_lengths(jax.random.fold_in(streams_of[6], 71), 0),
        "rewards": plant(jax.random.randint(streams_of[5], (PROMPTS, RESP), 0, 4), jax.random.fold_in(streams_of[5], 1), 0, 3).astype(jnp.int32),
    }


def reference(hidden_in, gain, value_weight, value_cot, lengths, rewards):
    scores = rewards.astype(jnp.float32)
    centre = lax.optimization_barrier(jnp.sum(scores, axis=1, keepdims=True)) / RESP
    spread = lax.optimization_barrier(jnp.sum(scores * scores, axis=1, keepdims=True)) / RESP - centre * centre
    advantage = (scores - centre) / jnp.maximum(jnp.sqrt(spread), 1.0)
    position = jnp.arange(L)
    alive_mask = position[None, None, :] < lengths[:, :, None]
    token_weight = jnp.where(alive_mask, (advantage / lengths.astype(jnp.float32))[:, :, None], 0.0)
    flat_in = hidden_in.reshape(PROMPTS * RESP, L, D)
    flat_weight = token_weight.reshape(PROMPTS * RESP, L)
    flat_cot = value_cot.reshape(PROMPTS * RESP, L, KVW)

    def one_response(running, items):
        inputs, weights_row, cotangent = items
        widened = inputs.astype(jnp.float32)
        inverse = lax.rsqrt(lax.optimization_barrier(jnp.mean(widened * widened, axis=1, keepdims=True)) + 1e-06)
        unit = widened * inverse
        normed = (unit * gain).astype(jnp.bfloat16)
        projected = jnp.dot(normed, value_weight, preferred_element_type=jnp.float32).astype(jnp.bfloat16)
        scaled_cot = (weights_row[:, None] * cotangent.astype(jnp.float32)).astype(jnp.bfloat16)
        back = lax.dot_general(scaled_cot, value_weight, (((1,), (1,)), ((), ())), preferred_element_type=jnp.float32)
        gain_total = running[1] + lax.optimization_barrier(jnp.sum(back * unit, axis=0))
        grad_total = running[0] + lax.dot_general(normed, scaled_cot, (((0,), (0,)), ((), ())), preferred_element_type=jnp.float32)
        return ((grad_total, gain_total), projected)
    start_state = (jnp.zeros((D, KVW), jnp.float32), jnp.zeros((D,), jnp.float32))
    (weight_grad, gain_grad), values = lax.scan(one_response, start_state, (flat_in, flat_weight, flat_cot))
    return (values.reshape(PROMPTS, RESP, L, KVW), weight_grad, gain_grad)
```

```python
import jax
import jax.numpy as jnp
from jax import lax
from jax.sharding import PartitionSpec as P


def body(hidden_in, gain, value_weight, value_cot, lengths, rewards):
    prompts, answers, length, features = hidden_in.shape
    kv_width = value_weight.shape[1]
    row_count = prompts * answers * length
    n_dp = lax.axis_size("dp")
    n_group = lax.axis_size("group")
    group_count = answers * n_group
    shard_rows = value_weight.shape[0]
    scores = rewards.astype(jnp.float32)
    reward_sum, square_sum = lax.psum(
        (jnp.sum(scores, axis=1, keepdims=True), jnp.sum(scores * scores, axis=1, keepdims=True)),
        "group",
    )
    centre = reward_sum / group_count
    spread = square_sum / group_count - centre * centre
    advantage = (scores - centre) / jnp.maximum(jnp.sqrt(spread), 1.0)
    position = jnp.arange(length)
    alive_mask = position[None, None, :] < lengths[:, :, None]
    token_weight = jnp.where(alive_mask, (advantage / lengths.astype(jnp.float32))[:, :, None], 0.0)
    flat_in = hidden_in.reshape(row_count, features)
    inverse = lax.rsqrt(
        jnp.mean(jnp.square(flat_in.astype(jnp.float32)), axis=1, keepdims=True) + 1e-06
    )
    normed = (flat_in.astype(jnp.float32) * inverse * gain).astype(jnp.bfloat16)
    scaled_cot = (
        token_weight.reshape(row_count, 1)
        * value_cot.reshape(row_count, kv_width).astype(jnp.float32)
    ).astype(jnp.bfloat16)
    part = lax.all_gather(value_weight[None], "group", axis=0, tiled=True)
    full_weight = lax.all_gather(part[None], "dp", axis=0, tiled=True).reshape(features, kv_width)
    projected = jnp.dot(normed, full_weight, preferred_element_type=jnp.float32)
    back = lax.dot_general(
        scaled_cot, full_weight, (((1,), (1,)), ((), ())), preferred_element_type=jnp.float32
    )
    gain_term = jnp.sum(back * (flat_in.astype(jnp.float32) * inverse), axis=0)
    values = projected.astype(jnp.bfloat16).reshape(prompts, answers, length, kv_width)
    grad_part = lax.dot_general(
        normed, scaled_cot, (((0,), (0,)), ((), ())), preferred_element_type=jnp.float32
    )
    block = shard_rows * kv_width
    pad = (-shard_rows) % 128
    payload = jnp.concatenate(
        [
            grad_part.reshape(n_dp, n_group, block),
            jnp.pad(gain_term.reshape(n_dp, n_group, shard_rows), ((0, 0), (0, 0), (0, pad))),
        ],
        axis=2,
    )
    payload = lax.psum_scatter(payload, "dp", scatter_dimension=0, tiled=True)
    payload = lax.psum_scatter(payload.reshape(n_group, -1), "group", scatter_dimension=0, tiled=True)
    weight_grad = payload[0, :block].reshape(shard_rows, kv_width)
    gain_grad = payload[0, block:block + shard_rows]
    return (values, weight_grad, gain_grad)


def solution(mesh):
    in_specs = (
        P("dp", "group", None, None),
        P(),
        P(("dp", "group"), None),
        P("dp", "group", None, None),
        P("dp", "group"),
        P("dp", "group"),
    )
    out_specs = (P("dp", "group", None, None), P(("dp", "group"), None), P(("dp", "group")))
    return jax.shard_map(body, mesh=mesh, in_specs=in_specs, out_specs=out_specs, check_vma=False)
```

```python
import jax
import jax.numpy as jnp
from jax import lax
from jax.sharding import PartitionSpec as P


def body(hidden_in, gain, value_weight, value_cot, lengths, rewards):
    prompts, answers, length, features = hidden_in.shape
    kv_width = value_weight.shape[1]
    row_count = prompts * answers * length
    n_dp = lax.axis_size("dp")
    n_group = lax.axis_size("group")
    group_count = answers * n_group
    shard_rows = value_weight.shape[0]
    scores = rewards.astype(jnp.float32)
    reward_sum, square_sum = lax.psum(
        (jnp.sum(scores, axis=1, keepdims=True), jnp.sum(scores * scores, axis=1, keepdims=True)),
        "group",
    )
    centre = reward_sum / group_count
    spread = square_sum / group_count - centre * centre
    advantage = (scores - centre) / jnp.maximum(jnp.sqrt(spread), 1.0)
    position = jnp.arange(length)
    alive_mask = position[None, None, :] < lengths[:, :, None]
    token_weight = jnp.where(alive_mask, (advantage / lengths.astype(jnp.float32))[:, :, None], 0.0)
    flat_in = hidden_in.reshape(row_count, features)
    inverse = lax.rsqrt(
        jnp.mean(jnp.square(flat_in.astype(jnp.float32)), axis=1, keepdims=True) + 1e-06
    )
    normed = (flat_in.astype(jnp.float32) * inverse * gain).astype(jnp.bfloat16)
    scaled_cot = (
        token_weight.reshape(row_count, 1)
        * value_cot.reshape(row_count, kv_width).astype(jnp.float32)
    ).astype(jnp.bfloat16)
    part = lax.all_gather(value_weight[None], "group", axis=0, tiled=True)
    full_weight = lax.all_gather(part[None], "dp", axis=0, tiled=True).reshape(features, kv_width)
    projected = jnp.dot(normed, full_weight, preferred_element_type=jnp.float32)
    back = lax.dot_general(
        scaled_cot, full_weight, (((1,), (1,)), ((), ())), preferred_element_type=jnp.float32
    )
    gain_term = jnp.sum(back * (flat_in.astype(jnp.float32) * inverse), axis=0)
    values = projected.astype(jnp.bfloat16).reshape(prompts, answers, length, kv_width)
    grad_part = lax.dot_general(
        normed, scaled_cot, (((0,), (0,)), ((), ())), preferred_element_type=jnp.float32
    )
    block = shard_rows * kv_width
    pad = (-shard_rows) % 128
    payload = jnp.concatenate(
        [
            grad_part.reshape(n_dp, n_group, block),
            jnp.pad(gain_term.reshape(n_dp, n_group, shard_rows), ((0, 0), (0, 0), (0, pad))),
        ],
        axis=2,
    )
    payload = lax.psum_scatter(payload, "dp", scatter_dimension=0, tiled=True)
    payload = lax.all_to_all(payload.reshape(n_group, -1), "group", 0, 0, tiled=True).sum(0)
    weight_grad = payload[:block].reshape(shard_rows, kv_width)
    gain_grad = payload[block:block + shard_rows]
    return (values, weight_grad, gain_grad)


def solution(mesh):
    in_specs = (
        P("dp", "group", None, None),
        P(),
        P(("dp", "group"), None),
        P("dp", "group", None, None),
        P("dp", "group"),
        P("dp", "group"),
    )
    out_specs = (P("dp", "group", None, None), P(("dp", "group"), None), P(("dp", "group")))
    return jax.shard_map(body, mesh=mesh, in_specs=in_specs, out_specs=out_specs, check_vma=False)
```

```python
import jax
import jax.numpy as jnp
from jax import lax
from jax.sharding import PartitionSpec as P


def body(hidden_in, gain, value_weight, value_cot, lengths, rewards):
    prompts, answers, length, features = hidden_in.shape
    kv_width = value_weight.shape[1]
    row_count = prompts * answers * length
    n_dp = lax.axis_size("dp")
    n_group = lax.axis_size("group")
    group_count = answers * n_group
    shard_rows = value_weight.shape[0]
    scores = rewards.astype(jnp.float32)
    reward_sum, square_sum = lax.psum(
        (jnp.sum(scores, axis=1, keepdims=True), jnp.sum(scores * scores, axis=1, keepdims=True)),
        "group",
    )
    centre = reward_sum / group_count
    spread = square_sum / group_count - centre * centre
    advantage = (scores - centre) / jnp.maximum(jnp.sqrt(spread), 1.0)
    position = jnp.arange(length)
    alive_mask = position[None, None, :] < lengths[:, :, None]
    token_weight = jnp.where(alive_mask, (advantage / lengths.astype(jnp.float32))[:, :, None], 0.0)
    flat_in = hidden_in.reshape(row_count, features)
    inverse = lax.rsqrt(
        jnp.mean(jnp.square(flat_in.astype(jnp.float32)), axis=1, keepdims=True) + 1e-06
    )
    normed = (flat_in.astype(jnp.float32) * inverse * gain).astype(jnp.bfloat16)
    scaled_cot = (
        token_weight.reshape(row_count, 1)
        * value_cot.reshape(row_count, kv_width).astype(jnp.float32)
    ).astype(jnp.bfloat16)
    part = lax.all_gather(value_weight, "group", axis=0, tiled=True)
    full_weight = lax.all_gather(part, "dp", axis=0, tiled=True)
    projected = jnp.dot(normed, full_weight, preferred_element_type=jnp.float32)
    back = lax.dot_general(
        scaled_cot, full_weight, (((1,), (1,)), ((), ())), preferred_element_type=jnp.float32
    )
    gain_term = jnp.sum(back * (flat_in.astype(jnp.float32) * inverse), axis=0)
    values = projected.astype(jnp.bfloat16).reshape(prompts, answers, length, kv_width)
    grad_part = lax.dot_general(
        normed, scaled_cot, (((0,), (0,)), ((), ())), preferred_element_type=jnp.float32
    )
    grad_part = lax.psum_scatter(
        grad_part.reshape(n_dp, features // n_dp, kv_width), "dp", scatter_dimension=0, tiled=True
    )
    grad_part = grad_part.reshape(n_group, shard_rows, kv_width)
    weight_grad = lax.all_to_all(grad_part, "group", 0, 0, tiled=True).sum(0)
    gain_part = lax.all_to_all(gain_term.reshape(n_dp, features // n_dp), "dp", 0, 0, tiled=True)
    gain_part = gain_part.sum(0).reshape(n_group, shard_rows)
    gain_grad = lax.all_to_all(gain_part, "group", 0, 0, tiled=True).sum(0)
    return (values, weight_grad, gain_grad)


def solution(mesh):
    in_specs = (
        P("dp", "group", None, None),
        P(),
        P(("dp", "group"), None),
        P("dp", "group", None, None),
        P("dp", "group"),
        P("dp", "group"),
    )
    out_specs = (P("dp", "group", None, None), P(("dp", "group"), None), P(("dp", "group")))
    return jax.shard_map(body, mesh=mesh, in_specs=in_specs, out_specs=out_specs, check_vma=False)
```

```python
import jax
import jax.numpy as jnp
from jax import lax
from jax.sharding import PartitionSpec as P


def body(hidden_in, gain, value_weight, value_cot, lengths, rewards):
    prompts, answers, length, features = hidden_in.shape
    kv_width = value_weight.shape[1]
    row_count = prompts * answers * length
    n_dp = lax.axis_size("dp")
    n_group = lax.axis_size("group")
    group_count = answers * n_group
    shard_rows = value_weight.shape[0]
    scores = rewards.astype(jnp.float32)
    peer_scores = lax.all_to_all(
        jnp.broadcast_to(scores.reshape(1, -1), (n_group, scores.size)), "group", 0, 0, tiled=True
    )
    reward_sum = jnp.sum(peer_scores).reshape(1, 1)
    square_sum = jnp.sum(peer_scores * peer_scores).reshape(1, 1)
    centre = reward_sum / group_count
    spread = square_sum / group_count - centre * centre
    advantage = (scores - centre) / jnp.maximum(jnp.sqrt(spread), 1.0)
    position = jnp.arange(length)
    alive_mask = position[None, None, :] < lengths[:, :, None]
    token_weight = jnp.where(alive_mask, (advantage / lengths.astype(jnp.float32))[:, :, None], 0.0)
    flat_in = hidden_in.reshape(row_count, features)
    inverse = lax.rsqrt(
        jnp.mean(jnp.square(flat_in.astype(jnp.float32)), axis=1, keepdims=True) + 1e-06
    )
    normed = (flat_in.astype(jnp.float32) * inverse * gain).astype(jnp.bfloat16)
    scaled_cot = (
        token_weight.reshape(row_count, 1)
        * value_cot.reshape(row_count, kv_width).astype(jnp.float32)
    ).astype(jnp.bfloat16)
    part = lax.all_gather(value_weight, "group", axis=0, tiled=True)
    full_weight = lax.all_gather(part, "dp", axis=0, tiled=True)
    projected = jnp.dot(normed, full_weight, preferred_element_type=jnp.float32)
    back = lax.dot_general(
        scaled_cot, full_weight, (((1,), (1,)), ((), ())), preferred_element_type=jnp.float32
    )
    gain_term = jnp.sum(back * (flat_in.astype(jnp.float32) * inverse), axis=0)
    values = projected.astype(jnp.bfloat16).reshape(prompts, answers, length, kv_width)
    grad_part = lax.dot_general(
        normed, scaled_cot, (((0,), (0,)), ((), ())), preferred_element_type=jnp.float32
    )
    grad_part = lax.psum_scatter(
        grad_part.reshape(n_dp, features // n_dp, kv_width), "dp", scatter_dimension=0, tiled=True
    )
    grad_part = grad_part.reshape(n_group, shard_rows, kv_width)
    weight_grad = lax.all_to_all(grad_part, "group", 0, 0, tiled=True).sum(0)
    gain_part = lax.all_to_all(gain_term.reshape(n_dp, features // n_dp), "dp", 0, 0, tiled=True)
    gain_part = gain_part.sum(0).reshape(n_group, shard_rows)
    gain_grad = lax.all_to_all(gain_part, "group", 0, 0, tiled=True).sum(0)
    return (values, weight_grad, gain_grad)


def solution(mesh):
    in_specs = (
        P("dp", "group", None, None),
        P(),
        P(("dp", "group"), None),
        P("dp", "group", None, None),
        P("dp", "group"),
        P("dp", "group"),
    )
    out_specs = (P("dp", "group", None, None), P(("dp", "group"), None), P(("dp", "group")))
    return jax.shard_map(body, mesh=mesh, in_specs=in_specs, out_specs=out_specs, check_vma=False)
```

```python
import jax
import jax.numpy as jnp
from jax import lax
from jax.sharding import PartitionSpec as P


def body(hidden_in, gain, value_weight, value_cot, lengths, rewards):
    prompts, answers, length, features = hidden_in.shape
    kv_width = value_weight.shape[1]
    row_count = prompts * answers * length
    n_dp = lax.axis_size("dp")
    n_group = lax.axis_size("group")
    group_count = answers * n_group
    shard_rows = value_weight.shape[0]
    scores = rewards.astype(jnp.float32)
    peer_scores = lax.all_to_all(
        jnp.broadcast_to(scores.reshape(1, -1), (n_group, scores.size)), "group", 0, 0, tiled=True
    )
    reward_sum = jnp.sum(peer_scores).reshape(1, 1)
    square_sum = jnp.sum(peer_scores * peer_scores).reshape(1, 1)
    centre = reward_sum / group_count
    spread = square_sum / group_count - centre * centre
    advantage = (scores - centre) / jnp.maximum(jnp.sqrt(spread), 1.0)
    position = jnp.arange(length)
    alive_mask = position[None, None, :] < lengths[:, :, None]
    token_weight = jnp.where(alive_mask, (advantage / lengths.astype(jnp.float32))[:, :, None], 0.0)
    flat_in = hidden_in.reshape(row_count, features)
    inverse = lax.rsqrt(
        jnp.mean(jnp.square(flat_in.astype(jnp.float32)), axis=1, keepdims=True) + 1e-06
    )
    normed = (flat_in.astype(jnp.float32) * inverse * gain).astype(jnp.bfloat16)
    scaled_cot = (
        token_weight.reshape(row_count, 1)
        * value_cot.reshape(row_count, kv_width).astype(jnp.float32)
    ).astype(jnp.bfloat16)
    part = lax.all_to_all(
        jnp.broadcast_to(value_weight[None], (n_group,) + value_weight.shape), "group", 0, 0, tiled=True
    ).reshape(n_group * shard_rows, kv_width)
    full_weight = lax.all_gather(part, "dp", axis=0, tiled=True)
    projected = jnp.dot(normed, full_weight, preferred_element_type=jnp.float32)
    back = lax.dot_general(
        scaled_cot, full_weight, (((1,), (1,)), ((), ())), preferred_element_type=jnp.float32
    )
    gain_term = jnp.sum(back * (flat_in.astype(jnp.float32) * inverse), axis=0)
    values = projected.astype(jnp.bfloat16).reshape(prompts, answers, length, kv_width)
    grad_part = lax.dot_general(
        normed, scaled_cot, (((0,), (0,)), ((), ())), preferred_element_type=jnp.float32
    )
    grad_part = lax.psum_scatter(
        grad_part.reshape(n_dp, features // n_dp, kv_width), "dp", scatter_dimension=0, tiled=True
    )
    grad_part = grad_part.reshape(n_group, shard_rows, kv_width)
    weight_grad = lax.all_to_all(grad_part, "group", 0, 0, tiled=True).sum(0)
    gain_part = lax.all_to_all(gain_term.reshape(n_dp, features // n_dp), "dp", 0, 0, tiled=True)
    gain_part = gain_part.sum(0).reshape(n_group, shard_rows)
    gain_grad = lax.all_to_all(gain_part, "group", 0, 0, tiled=True).sum(0)
    return (values, weight_grad, gain_grad)


def solution(mesh):
    in_specs = (
        P("dp", "group", None, None),
        P(),
        P(("dp", "group"), None),
        P("dp", "group", None, None),
        P("dp", "group"),
        P("dp", "group"),
    )
    out_specs = (P("dp", "group", None, None), P(("dp", "group"), None), P(("dp", "group")))
    return jax.shard_map(body, mesh=mesh, in_specs=in_specs, out_specs=out_specs, check_vma=False)
```

```python
import jax
import jax.numpy as jnp
from jax import lax
from jax.sharding import PartitionSpec as P


def body(hidden_in, gain, value_weight, value_cot, lengths, rewards):
    prompts, answers, length, features = hidden_in.shape
    kv_width = value_weight.shape[1]
    row_count = prompts * answers * length
    n_dp = lax.axis_size("dp")
    n_group = lax.axis_size("group")
    group_count = answers * n_group
    shard_rows = value_weight.shape[0]
    scores = rewards.astype(jnp.float32)
    peer_scores = lax.all_to_all(
        jnp.broadcast_to(scores.reshape(1, -1), (n_group, scores.size)), "group", 0, 0, tiled=True
    )
    reward_sum = jnp.sum(peer_scores).reshape(1, 1)
    square_sum = jnp.sum(peer_scores * peer_scores).reshape(1, 1)
    centre = reward_sum / group_count
    spread = square_sum / group_count - centre * centre
    advantage = (scores - centre) / jnp.maximum(jnp.sqrt(spread), 1.0)
    position = jnp.arange(length)
    alive_mask = position[None, None, :] < lengths[:, :, None]
    token_weight = jnp.where(alive_mask, (advantage / lengths.astype(jnp.float32))[:, :, None], 0.0)
    flat_in = hidden_in.reshape(row_count, features)
    inverse = lax.rsqrt(
        jnp.mean(jnp.square(flat_in.astype(jnp.float32)), axis=1, keepdims=True) + 1e-06
    )
    normed = (flat_in.astype(jnp.float32) * inverse * gain).astype(jnp.bfloat16)
    scaled_cot = (
        token_weight.reshape(row_count, 1)
        * value_cot.reshape(row_count, kv_width).astype(jnp.float32)
    ).astype(jnp.bfloat16)
    part = lax.all_to_all(
        jnp.broadcast_to(value_weight[None], (n_group,) + value_weight.shape), "group", 0, 0, tiled=True
    ).reshape(n_group * shard_rows, kv_width)
    full_weight = lax.all_gather(part, "dp", axis=0, tiled=True)
    projected = jnp.dot(normed, full_weight, preferred_element_type=jnp.float32)
    back = lax.dot_general(
        scaled_cot, full_weight, (((1,), (1,)), ((), ())), preferred_element_type=jnp.float32
    )
    gain_term = jnp.sum(back * (flat_in.astype(jnp.float32) * inverse), axis=0)
    values = projected.astype(jnp.bfloat16).reshape(prompts, answers, length, kv_width)
    grad_part = lax.dot_general(
        normed, scaled_cot, (((0,), (0,)), ((), ())), preferred_element_type=jnp.float32
    )
    grad_part = lax.psum_scatter(
        grad_part.reshape(n_dp, features // n_dp, kv_width).astype(jnp.bfloat16),
        "dp",
        scatter_dimension=0,
        tiled=True,
    )
    grad_part = grad_part.astype(jnp.float32).reshape(n_group, shard_rows, kv_width)
    weight_grad = lax.all_to_all(grad_part, "group", 0, 0, tiled=True).sum(0)
    gain_part = lax.all_to_all(gain_term.reshape(n_dp, features // n_dp), "dp", 0, 0, tiled=True)
    gain_part = gain_part.sum(0).reshape(n_group, shard_rows)
    gain_grad = lax.all_to_all(gain_part, "group", 0, 0, tiled=True).sum(0)
    return (values, weight_grad, gain_grad)


def solution(mesh):
    in_specs = (
        P("dp", "group", None, None),
        P(),
        P(("dp", "group"), None),
        P("dp", "group", None, None),
        P("dp", "group"),
        P("dp", "group"),
    )
    out_specs = (P("dp", "group", None, None), P(("dp", "group"), None), P(("dp", "group")))
    return jax.shard_map(body, mesh=mesh, in_specs=in_specs, out_specs=out_specs, check_vma=False)
```

```python
import jax
import jax.numpy as jnp
from jax import lax
from jax.sharding import PartitionSpec as P


def body(hidden_in, gain, value_weight, value_cot, lengths, rewards):
    prompts, answers, length, features = hidden_in.shape
    kv_width = value_weight.shape[1]
    row_count = prompts * answers * length
    n_dp = lax.axis_size("dp")
    n_group = lax.axis_size("group")
    group_count = answers * n_group
    shard_rows = value_weight.shape[0]
    scores = rewards.astype(jnp.float32)
    peer_scores = lax.all_to_all(
        jnp.broadcast_to(scores.reshape(1, -1), (n_group, scores.size)), "group", 0, 0, tiled=True
    )
    reward_sum = jnp.sum(peer_scores).reshape(1, 1)
    square_sum = jnp.sum(peer_scores * peer_scores).reshape(1, 1)
    centre = reward_sum / group_count
    spread = square_sum / group_count - centre * centre
    advantage = (scores - centre) / jnp.maximum(jnp.sqrt(spread), 1.0)
    position = jnp.arange(length)
    alive_mask = position[None, None, :] < lengths[:, :, None]
    token_weight = jnp.where(alive_mask, (advantage / lengths.astype(jnp.float32))[:, :, None], 0.0)
    flat_in = hidden_in.reshape(row_count, features)
    inverse = lax.rsqrt(
        jnp.mean(jnp.square(flat_in.astype(jnp.float32)), axis=1, keepdims=True) + 1e-06
    )
    normed = (flat_in.astype(jnp.float32) * inverse * gain).astype(jnp.bfloat16)
    scaled_cot = (
        token_weight.reshape(row_count, 1)
        * value_cot.reshape(row_count, kv_width).astype(jnp.float32)
    ).astype(jnp.bfloat16)
    part = lax.all_to_all(
        jnp.broadcast_to(value_weight[None], (n_group,) + value_weight.shape), "group", 0, 0, tiled=True
    ).reshape(n_group * shard_rows, kv_width)
    full_weight = lax.all_gather(part, "dp", axis=0, tiled=True)
    projected = jnp.dot(normed, full_weight, preferred_element_type=jnp.float32)
    back = lax.dot_general(
        scaled_cot, full_weight, (((1,), (1,)), ((), ())), preferred_element_type=jnp.float32
    )
    gain_term = jnp.sum(back * (flat_in.astype(jnp.float32) * inverse), axis=0)
    values = projected.astype(jnp.bfloat16).reshape(prompts, answers, length, kv_width)
    half = kv_width // 2
    grad_halves = []
    for lo in (0, half):
        grad_part = lax.dot_general(
            normed, scaled_cot[:, lo:lo + half], (((0,), (0,)), ((), ())), preferred_element_type=jnp.float32
        )
        grad_part = lax.psum_scatter(
            grad_part.reshape(n_dp, features // n_dp, half), "dp", scatter_dimension=0, tiled=True
        )
        grad_part = grad_part.reshape(n_group, shard_rows, half)
        grad_halves.append(lax.all_to_all(grad_part, "group", 0, 0, tiled=True).sum(0))
    weight_grad = jnp.concatenate(grad_halves, axis=1)
    gain_part = lax.all_to_all(gain_term.reshape(n_dp, features // n_dp), "dp", 0, 0, tiled=True)
    gain_part = gain_part.sum(0).reshape(n_group, shard_rows)
    gain_grad = lax.all_to_all(gain_part, "group", 0, 0, tiled=True).sum(0)
    return (values, weight_grad, gain_grad)


def solution(mesh):
    in_specs = (
        P("dp", "group", None, None),
        P(),
        P(("dp", "group"), None),
        P("dp", "group", None, None),
        P("dp", "group"),
        P("dp", "group"),
    )
    out_specs = (P("dp", "group", None, None), P(("dp", "group"), None), P(("dp", "group")))
    return jax.shard_map(body, mesh=mesh, in_specs=in_specs, out_specs=out_specs, check_vma=False)
```

```python
import jax
import jax.numpy as jnp
from jax import lax
from jax.sharding import PartitionSpec as P


def body(hidden_in, gain, value_weight, value_cot, lengths, rewards):
    prompts, answers, length, features = hidden_in.shape
    kv_width = value_weight.shape[1]
    row_count = prompts * answers * length
    n_dp = lax.axis_size("dp")
    n_group = lax.axis_size("group")
    group_count = answers * n_group
    shard_rows = value_weight.shape[0]
    scores = rewards.astype(jnp.float32)
    peer_scores = lax.all_to_all(
        jnp.broadcast_to(scores.reshape(1, -1), (n_group, scores.size)), "group", 0, 0, tiled=True
    )
    reward_sum = jnp.sum(peer_scores).reshape(1, 1)
    square_sum = jnp.sum(peer_scores * peer_scores).reshape(1, 1)
    centre = reward_sum / group_count
    spread = square_sum / group_count - centre * centre
    advantage = (scores - centre) / jnp.maximum(jnp.sqrt(spread), 1.0)
    position = jnp.arange(length)
    alive_mask = position[None, None, :] < lengths[:, :, None]
    token_weight = jnp.where(alive_mask, (advantage / lengths.astype(jnp.float32))[:, :, None], 0.0)
    flat_in = hidden_in.reshape(row_count, features)
    inverse = lax.rsqrt(
        jnp.mean(jnp.square(flat_in.astype(jnp.float32)), axis=1, keepdims=True) + 1e-06
    )
    normed = (flat_in.astype(jnp.float32) * inverse * gain).astype(jnp.bfloat16)
    scaled_cot = (
        token_weight.reshape(row_count, 1)
        * value_cot.reshape(row_count, kv_width).astype(jnp.float32)
    ).astype(jnp.bfloat16)
    part = lax.all_to_all(
        jnp.broadcast_to(value_weight[None], (n_group,) + value_weight.shape), "group", 0, 0, tiled=True
    ).reshape(n_group * shard_rows, kv_width)
    full_weight = lax.all_gather(part, "dp", axis=0, tiled=True)
    projected = jnp.dot(normed, full_weight, preferred_element_type=jnp.float32)
    back = lax.dot_general(
        scaled_cot, full_weight, (((1,), (1,)), ((), ())), preferred_element_type=jnp.float32
    )
    gain_term = jnp.sum(back * (flat_in.astype(jnp.float32) * inverse), axis=0)
    values = projected.astype(jnp.bfloat16).reshape(prompts, answers, length, kv_width)
    grad_part = lax.dot_general(
        normed, scaled_cot, (((0,), (0,)), ((), ())), preferred_element_type=jnp.float32
    )
    grad_part = lax.psum_scatter(
        grad_part.reshape(n_dp, features // n_dp, kv_width), "dp", scatter_dimension=0, tiled=True
    )
    grad_part = grad_part.reshape(n_group, shard_rows, kv_width)
    weight_grad = lax.all_to_all(grad_part.astype(jnp.bfloat16), "group", 0, 0, tiled=True)
    weight_grad = weight_grad.astype(jnp.float32).sum(0)
    gain_part = lax.all_to_all(gain_term.reshape(n_dp, features // n_dp), "dp", 0, 0, tiled=True)
    gain_part = gain_part.sum(0).reshape(n_group, shard_rows)
    gain_grad = lax.all_to_all(gain_part, "group", 0, 0, tiled=True).sum(0)
    return (values, weight_grad, gain_grad)


def solution(mesh):
    in_specs = (
        P("dp", "group", None, None),
        P(),
        P(("dp", "group"), None),
        P("dp", "group", None, None),
        P("dp", "group"),
        P("dp", "group"),
    )
    out_specs = (P("dp", "group", None, None), P(("dp", "group"), None), P(("dp", "group")))
    return jax.shard_map(body, mesh=mesh, in_specs=in_specs, out_specs=out_specs, check_vma=False)
```
